1024 devices in a mesh: dp: 16 (over z_lo, x), space: 64 (over y, z_hi, core).
Axes of the slice: x: 4, y: 8, z: 16 (z_hi: 4, z_lo: 4; z = z_hi * 4 + z_lo), core: 2. Of those that a mesh axis runs over, the one named last changes fastest.
Arguments:
- volume: bfloat16 [16, 32, 128, 16, 128], P('dp', None, 'space'), may hold values from -6 to 6
- kernel: bfloat16 [64, 32, 3, 3, 3], replicated, may hold values from -0.21875 to 0.21875
- cotangent: bfloat16 [16, 64, 64, 8, 64], P('dp', None, 'space'), may hold values from -6 to 6
Outputs:
- activated: bfloat16 [16, 64, 64, 8, 64], P('dp', None, 'space')
- grad_volume: bfloat16 [16, 32, 128, 16, 128], P('dp', None, 'space')
- grad_kernel: float32 [64, 32, 3, 3, 3], replicated
The draws below stay inside these ranges and needn't reach their ends.
All inputs are finite; a program needn't handle non-finite values.
Results may differ from the reference program's by a relative error of at most 0.0049.
Values may be sent and summed in bfloat16 or wider, within the bound.
No kernel may reach another device: no remote copies, remote signals or barrier semaphores. Data moves between devices by JAX's collectives and lax.ppermute only.
A program may use at most 64 MiB of HBM per device.

```python
import jax
import jax.numpy as jnp
from jax import lax

CIN = 32
COUT = 64
GY = 16
GZ = 128
SAMPLES = 16
GX = 128


def levels(own_key, extent, split, low, high):
    factor_of, own = 1.0, jax.random.fold_in(own_key, 6)
    for dim, shards_of in split:
        steps = jnp.exp(jax.random.uniform(jax.random.fold_in(own, dim), (shards_of,), jnp.float32, low / len(split), high / len(split)))
        factor_of = factor_of * jnp.repeat(steps, extent[dim] // shards_of).reshape([-1 if axis == dim else 1 for axis in range(len(extent))])
    return factor_of


def noise(key, dims, width, limit, cuts=(), dtype=jnp.bfloat16):
    entries = width * jax.random.normal(key, dims, jnp.float32)
    if cuts:
        entries = entries * levels(key, dims, cuts, -0.22, 0.18)
    return jnp.clip(entries, -limit, limit).astype(dtype)


def setup_inputs(seed: int = 0) -> dict:
    splits = jax.random.split(jax.random.key(seed), 4)
    return {
        "volume": noise(splits[0], (SAMPLES, CIN, GX, GY, GZ), 1.0, 6.0, ((0, 16), (2, 64))),
        "kernel": noise(splits[1], (COUT, CIN, 3, 3, 3), (27 * CIN) ** -0.5, 0.21875),
        "cotangent": noise(splits[2], (SAMPLES, COUT, GX // 2, GY // 2, GZ // 2), 1.0, 6.0, ((0, 16), (2, 64))),
    }


def convolve(inputs, weights, precision):
    return lax.conv_general_dilated(inputs, weights, (2, 2, 2), [(1, 1), (1, 1), (1, 1)], dimension_numbers=('NCDHW', 'OIDHW', 'NCDHW'), preferred_element_type=jnp.float32, precision=precision)

def reference(volume, kernel, cotangent):
    pre = convolve(volume, kernel, None)
    activated = (0.01 * pre + 0.99 * jax.nn.softplus(pre)).astype(jnp.bfloat16)
    local_grad = (cotangent.astype(jnp.float32) * (0.01 + 0.99 * jax.nn.sigmoid(pre))).astype(jnp.bfloat16)

    def full_conv(inputs, weights):
        return convolve(inputs, weights, lax.Precision.HIGHEST)
    unused, pullback = jax.vjp(full_conv, volume.astype(jnp.float32), kernel.astype(jnp.float32))
    grad_input, kernel_total = pullback(local_grad.astype(jnp.float32))
    count = SAMPLES * GX * GY * GZ / 8.0
    grad_kernel = kernel_total / jnp.sqrt(jnp.float32(count))
    return (activated, grad_input.astype(jnp.bfloat16), grad_kernel)
```

```python
import jax
import jax.numpy as jnp
from jax import lax
from jax.sharding import PartitionSpec as P


def from_behind(block, axis, distance):
    devices = range(lax.axis_size(axis))
    route = [(i - distance, i) for i in devices if i - distance in devices]
    return lax.ppermute(block, axis, route)


def in_blocks(x, dim, devices):
    dims = x.shape
    parts = x.reshape(*dims[:dim], devices, dims[dim] // devices, *dims[dim + 1 :])
    return jnp.moveaxis(parts, dim, 0)


def summed_on_arrival(x, axis, dim):
    parts = in_blocks(x, dim, lax.axis_size(axis))
    arrived = lax.all_to_all(parts, axis, split_axis=0, concat_axis=0, tiled=True)
    return arrived.sum(axis=0)


def sent_to_all(x, axis):
    copies = jnp.broadcast_to(x, (lax.axis_size(axis), *x.shape))
    return lax.all_to_all(copies, axis, split_axis=0, concat_axis=0, tiled=True)


def taken_together(x, axis):
    everything = sent_to_all(x, axis)
    return jnp.sum(everything, axis=0)


def laid_out(parts, dim):
    parts = jnp.moveaxis(parts, 0, dim)
    dims = parts.shape
    return parts.reshape(*dims[:dim], dims[dim] * dims[dim + 1], *dims[dim + 2 :])


def gathered_copies(x, axis, dim):
    parts = sent_to_all(x, axis)
    return laid_out(parts, dim)


def convolve(inputs, weights, low, high):
    return lax.conv_general_dilated(
        inputs,
        weights,
        (2, 2, 2),
        [(low, high), (1, 1), (1, 1)],
        dimension_numbers=("NCDHW", "OIDHW", "NCDHW"),
        preferred_element_type=jnp.float32,
    )


def input_grad(grads, weights, low, high):
    flipped = weights[:, :, ::-1, ::-1, ::-1]
    return lax.conv_general_dilated(
        grads,
        flipped,
        (1, 1, 1),
        [(low, high), (1, 2), (1, 2)],
        lhs_dilation=(2, 2, 2),
        dimension_numbers=("NCDHW", "IODHW", "NCDHW"),
        preferred_element_type=jnp.float32,
    )


def weight_grad(inputs, grads):
    return lax.conv_general_dilated(
        inputs,
        grads,
        (1, 1, 1),
        [(0, 0), (1, 0), (1, 0)],
        rhs_dilation=(2, 2, 2),
        dimension_numbers=("CNDHW", "IODHW", "CNDHW"),
        preferred_element_type=jnp.float32,
    )


def per_device(volume, kernel, cotangent):
    below = from_behind(volume[:, :, -1:], "space", 1)
    extended = jnp.concatenate([below, volume], axis=2)
    pre = convolve(extended, kernel, 0, 0)
    activated = (0.01 * pre + 0.99 * jax.nn.softplus(pre)).astype(jnp.bfloat16)
    local_grad = (cotangent.astype(jnp.float32) * (0.01 + 0.99 * jax.nn.sigmoid(pre))).astype(
        jnp.bfloat16
    )
    grad_extended = input_grad(local_grad, kernel, 2, 2)
    kernel_local = weight_grad(extended, local_grad)
    grad_input = grad_extended[:, :, 1:]
    next_grad = from_behind(local_grad[:, :, :1], "space", -1)
    from_above = input_grad(next_grad, kernel, 2, 0)
    grad_input = grad_input.at[:, :, -1:].add(from_above)
    kernel_total = lax.psum(kernel_local, ("dp", "space"))
    total_cells = (
        volume.shape[0]
        * lax.axis_size("dp")
        * volume.shape[2]
        * lax.axis_size("space")
        * volume.shape[3]
        * volume.shape[4]
        / 8.0
    )
    grad_kernel = kernel_total / jnp.sqrt(jnp.float32(total_cells))
    return (activated, grad_input.astype(jnp.bfloat16), grad_kernel)


def solution(mesh):
    placed = (P("dp", None, "space", None, None), P(), P("dp", None, "space", None, None))
    return jax.shard_map(
        per_device,
        mesh=mesh,
        in_specs=placed,
        out_specs=(P("dp", None, "space", None, None), P("dp", None, "space", None, None), P()),
        check_vma=False,
    )
```

```python
import jax
import jax.numpy as jnp
from jax import lax
from jax.sharding import PartitionSpec as P


def from_behind(block, axis, distance):
    devices = range(lax.axis_size(axis))
    route = [(i - distance, i) for i in devices if i - distance in devices]
    return lax.ppermute(block, axis, route)


def in_blocks(x, dim, devices):
    dims = x.shape
    parts = x.reshape(*dims[:dim], devices, dims[dim] // devices, *dims[dim + 1 :])
    return jnp.moveaxis(parts, dim, 0)


def summed_on_arrival(x, axis, dim):
    parts = in_blocks(x, dim, lax.axis_size(axis))
    arrived = lax.all_to_all(parts, axis, split_axis=0, concat_axis=0, tiled=True)
    return arrived.sum(axis=0)


def sent_to_all(x, axis):
    copies = jnp.broadcast_to(x, (lax.axis_size(axis), *x.shape))
    return lax.all_to_all(copies, axis, split_axis=0, concat_axis=0, tiled=True)


def taken_together(x, axis):
    everything = sent_to_all(x, axis)
    return jnp.sum(everything, axis=0)


def laid_out(parts, dim):
    parts = jnp.moveaxis(parts, 0, dim)
    dims = parts.shape
    return parts.reshape(*dims[:dim], dims[dim] * dims[dim + 1], *dims[dim + 2 :])


def gathered_copies(x, axis, dim):
    parts = sent_to_all(x, axis)
    return laid_out(parts, dim)


def convolve(inputs, weights, low, high):
    return lax.conv_general_dilated(
        inputs,
        weights,
        (2, 2, 2),
        [(low, high), (1, 1), (1, 1)],
        dimension_numbers=("NCDHW", "OIDHW", "NCDHW"),
        preferred_element_type=jnp.float32,
    )


def input_grad(grads, weights, low, high):
    flipped = weights[:, :, ::-1, ::-1, ::-1]
    return lax.conv_general_dilated(
        grads,
        flipped,
        (1, 1, 1),
        [(low, high), (1, 2), (1, 2)],
        lhs_dilation=(2, 2, 2),
        dimension_numbers=("NCDHW", "IODHW", "NCDHW"),
        preferred_element_type=jnp.float32,
    )


def weight_grad(inputs, grads):
    return lax.conv_general_dilated(
        inputs,
        grads,
        (1, 1, 1),
        [(0, 0), (1, 0), (1, 0)],
        rhs_dilation=(2, 2, 2),
        dimension_numbers=("CNDHW", "IODHW", "CNDHW"),
        preferred_element_type=jnp.float32,
    )


def patches(extended):
    planes, high, deep = extended.shape[2] - 1, extended.shape[3], extended.shape[4]
    padded = jnp.pad(extended[0], ((0, 0), (0, 0), (1, 0), (1, 0)))
    taps = [
        padded[:, a : a + planes : 2, b : b + high : 2, d : d + deep : 2]
        for a in range(3)
        for b in range(3)
        for d in range(3)
    ]
    cells = jnp.stack(taps, axis=1)
    return cells.reshape(cells.shape[0] * 27, -1)


def per_device(volume, kernel, cotangent):
    below = from_behind(volume[:, :, -1:], "space", 1)
    extended = jnp.concatenate([below, volume], axis=2)
    cells = patches(extended)
    weights = kernel.reshape(kernel.shape[0], -1)
    pre = jnp.dot(weights, cells, preferred_element_type=jnp.float32).reshape(cotangent.shape)
    activated = (0.01 * pre + 0.99 * jax.nn.softplus(pre)).astype(jnp.bfloat16)
    local_grad = (cotangent.astype(jnp.float32) * (0.01 + 0.99 * jax.nn.sigmoid(pre))).astype(
        jnp.bfloat16
    )
    grad_extended = input_grad(local_grad, kernel, 2, 2)
    kernel_local = jnp.dot(
        local_grad.reshape(local_grad.shape[1], -1), cells.T, preferred_element_type=jnp.float32
    ).reshape(kernel.shape)
    grad_input = grad_extended[:, :, 1:]
    next_grad = from_behind(local_grad[:, :, :1], "space", -1)
    from_above = input_grad(next_grad, kernel, 2, 0)
    grad_input = grad_input.at[:, :, -1:].add(from_above)
    flat_terms = kernel_local.reshape(-1)
    share = summed_on_arrival(flat_terms, "space", 0)
    share = taken_together(share, "dp")
    kernel_total = gathered_copies(share, "space", 0).reshape(kernel_local.shape)
    total_cells = (
        volume.shape[0]
        * lax.axis_size("dp")
        * volume.shape[2]
        * lax.axis_size("space")
        * volume.shape[3]
        * volume.shape[4]
        / 8.0
    )
    grad_kernel = kernel_total / jnp.sqrt(jnp.float32(total_cells))
    return (activated, grad_input.astype(jnp.bfloat16), grad_kernel)


def solution(mesh):
    placed = (P("dp", None, "space", None, None), P(), P("dp", None, "space", None, None))
    return jax.shard_map(
        per_device,
        mesh=mesh,
        in_specs=placed,
        out_specs=(P("dp", None, "space", None, None), P("dp", None, "space", None, None), P()),
        check_vma=False,
    )
```

```python
import jax
import jax.numpy as jnp
from jax import lax
from jax.sharding import PartitionSpec as P


def from_behind(block, axis, distance):
    devices = range(lax.axis_size(axis))
    route = [(i - distance, i) for i in devices if i - distance in devices]
    return lax.ppermute(block, axis, route)


def in_blocks(x, dim, devices):
    dims = x.shape
    parts = x.reshape(*dims[:dim], devices, dims[dim] // devices, *dims[dim + 1 :])
    return jnp.moveaxis(parts, dim, 0)


def summed_on_arrival(x, axis, dim):
    parts = in_blocks(x, dim, lax.axis_size(axis))
    arrived = lax.all_to_all(parts, axis, split_axis=0, concat_axis=0, tiled=True)
    return arrived.sum(axis=0)


def sent_to_all(x, axis):
    copies = jnp.broadcast_to(x, (lax.axis_size(axis), *x.shape))
    return lax.all_to_all(copies, axis, split_axis=0, concat_axis=0, tiled=True)


def taken_together(x, axis):
    everything = sent_to_all(x, axis)
    return jnp.sum(everything, axis=0)


def laid_out(parts, dim):
    parts = jnp.moveaxis(parts, 0, dim)
    dims = parts.shape
    return parts.reshape(*dims[:dim], dims[dim] * dims[dim + 1], *dims[dim + 2 :])


def gathered_copies(x, axis, dim):
    parts = sent_to_all(x, axis)
    return laid_out(parts, dim)


def convolve(inputs, weights, low, high):
    return lax.conv_general_dilated(
        inputs,
        weights,
        (2, 2, 2),
        [(low, high), (1, 1), (1, 1)],
        dimension_numbers=("NCDHW", "OIDHW", "NCDHW"),
        preferred_element_type=jnp.float32,
    )


def input_grad(grads, weights, low, high):
    flipped = weights[:, :, ::-1, ::-1, ::-1]
    return lax.conv_general_dilated(
        grads,
        flipped,
        (1, 1, 1),
        [(low, high), (1, 2), (1, 2)],
        lhs_dilation=(2, 2, 2),
        dimension_numbers=("NCDHW", "IODHW", "NCDHW"),
        preferred_element_type=jnp.float32,
    )


def weight_grad(inputs, grads):
    return lax.conv_general_dilated(
        inputs,
        grads,
        (1, 1, 1),
        [(0, 0), (1, 0), (1, 0)],
        rhs_dilation=(2, 2, 2),
        dimension_numbers=("CNDHW", "IODHW", "CNDHW"),
        preferred_element_type=jnp.float32,
    )


def patches(extended):
    planes, high, deep = extended.shape[2] - 1, extended.shape[3], extended.shape[4]
    channels = extended.shape[1]
    padded = jnp.pad(extended[0], ((0, 0), (0, 0), (1, 1), (1, 1)))
    split = padded.reshape(channels, planes + 1, high // 2 + 1, 2, deep // 2 + 1, 2)
    split = jnp.transpose(split, (0, 1, 3, 5, 2, 4))
    taps = [
        split[:, a : a + planes : 2, b % 2, d % 2, b // 2 : b // 2 + high // 2, d // 2 : d // 2 + deep // 2]
        for a in range(3)
        for b in range(3)
        for d in range(3)
    ]
    cells = jnp.stack(taps, axis=1)
    return cells.reshape(channels * 27, -1)

def per_device(volume, kernel, cotangent):
    below = from_behind(volume[:, :, -1:], "space", 1)
    extended = jnp.concatenate([below, volume], axis=2)
    cells = patches(extended)
    weights = kernel.reshape(kernel.shape[0], -1)
    pre = jnp.dot(weights, cells, preferred_element_type=jnp.float32).reshape(cotangent.shape)
    activated = (0.01 * pre + 0.99 * jax.nn.softplus(pre)).astype(jnp.bfloat16)
    local_grad = (cotangent.astype(jnp.float32) * (0.01 + 0.99 * jax.nn.sigmoid(pre))).astype(
        jnp.bfloat16
    )
    grad_extended = input_grad(local_grad, kernel, 2, 2)
    kernel_local = jnp.dot(
        local_grad.reshape(local_grad.shape[1], -1), cells.T, preferred_element_type=jnp.float32
    ).reshape(kernel.shape)
    grad_input = grad_extended[:, :, 1:]
    next_grad = from_behind(local_grad[:, :, :1], "space", -1)
    from_above = input_grad(next_grad, kernel, 2, 0)
    grad_input = grad_input.at[:, :, -1:].add(from_above)
    flat_terms = kernel_local.reshape(-1)
    share = summed_on_arrival(flat_terms, "space", 0)
    share = taken_together(share, "dp")
    kernel_total = gathered_copies(share, "space", 0).reshape(kernel_local.shape)
    total_cells = (
        volume.shape[0]
        * lax.axis_size("dp")
        * volume.shape[2]
        * lax.axis_size("space")
        * volume.shape[3]
        * volume.shape[4]
        / 8.0
    )
    grad_kernel = kernel_total / jnp.sqrt(jnp.float32(total_cells))
    return (activated, grad_input.astype(jnp.bfloat16), grad_kernel)


def solution(mesh):
    placed = (P("dp", None, "space", None, None), P(), P("dp", None, "space", None, None))
    return jax.shard_map(
        per_device,
        mesh=mesh,
        in_specs=placed,
        out_specs=(P("dp", None, "space", None, None), P("dp", None, "space", None, None), P()),
        check_vma=False,
    )
```

```python
import jax
import jax.numpy as jnp
from jax import lax
from jax.sharding import PartitionSpec as P


def from_behind(block, axis, distance):
    devices = range(lax.axis_size(axis))
    route = [(i - distance, i) for i in devices if i - distance in devices]
    return lax.ppermute(block, axis, route)


def in_blocks(x, dim, devices):
    dims = x.shape
    parts = x.reshape(*dims[:dim], devices, dims[dim] // devices, *dims[dim + 1 :])
    return jnp.moveaxis(parts, dim, 0)


def summed_on_arrival(x, axis, dim):
    parts = in_blocks(x, dim, lax.axis_size(axis))
    arrived = lax.all_to_all(parts.astype(jnp.bfloat16), axis, split_axis=0, concat_axis=0, tiled=True)
    return arrived.astype(jnp.float32).sum(axis=0)


def sent_to_all(x, axis):
    copies = jnp.broadcast_to(x, (lax.axis_size(axis), *x.shape))
    return lax.all_to_all(copies, axis, split_axis=0, concat_axis=0, tiled=True)


def taken_together(x, axis):
    everything = sent_to_all(x.astype(jnp.bfloat16), axis)
    return jnp.sum(everything.astype(jnp.float32), axis=0)


def laid_out(parts, dim):
    parts = jnp.moveaxis(parts, 0, dim)
    dims = parts.shape
    return parts.reshape(*dims[:dim], dims[dim] * dims[dim + 1], *dims[dim + 2 :])


def gathered_copies(x, axis, dim):
    parts = sent_to_all(x.astype(jnp.bfloat16), axis)
    return laid_out(parts.astype(jnp.float32), dim)


def convolve(inputs, weights, low, high):
    return lax.conv_general_dilated(
        inputs,
        weights,
        (2, 2, 2),
        [(low, high), (1, 1), (1, 1)],
        dimension_numbers=("NCDHW", "OIDHW", "NCDHW"),
        preferred_element_type=jnp.float32,
    )


def input_grad(grads, weights, low, high):
    flipped = weights[:, :, ::-1, ::-1, ::-1]
    return lax.conv_general_dilated(
        grads,
        flipped,
        (1, 1, 1),
        [(low, high), (1, 2), (1, 2)],
        lhs_dilation=(2, 2, 2),
        dimension_numbers=("NCDHW", "IODHW", "NCDHW"),
        preferred_element_type=jnp.float32,
    )


def weight_grad(inputs, grads):
    return lax.conv_general_dilated(
        inputs,
        grads,
        (1, 1, 1),
        [(0, 0), (1, 0), (1, 0)],
        rhs_dilation=(2, 2, 2),
        dimension_numbers=("CNDHW", "IODHW", "CNDHW"),
        preferred_element_type=jnp.float32,
    )


def per_device(volume, kernel, cotangent):
    below = from_behind(volume[:, :, -1:], "space", 1)
    extended = jnp.concatenate([below, volume], axis=2)
    pre = convolve(extended, kernel, 0, 0)
    activated = (0.01 * pre + 0.99 * jax.nn.softplus(pre)).astype(jnp.bfloat16)
    local_grad = (cotangent.astype(jnp.float32) * (0.01 + 0.99 * jax.nn.sigmoid(pre))).astype(
        jnp.bfloat16
    )
    grad_extended = input_grad(local_grad, kernel, 2, 2)
    kernel_local = weight_grad(extended, local_grad)
    grad_input = grad_extended[:, :, 1:]
    next_grad = from_behind(local_grad[:, :, :1], "space", -1)
    from_above = input_grad(next_grad, kernel, 2, 0)
    grad_input = grad_input.at[:, :, -1:].add(from_above)
    flat_terms = kernel_local.reshape(-1)
    share = summed_on_arrival(flat_terms, "space", 0)
    share = taken_together(share, "dp")
    kernel_total = gathered_copies(share, "space", 0).reshape(kernel_local.shape)
    total_cells = (
        volume.shape[0]
        * lax.axis_size("dp")
        * volume.shape[2]
        * lax.axis_size("space")
        * volume.shape[3]
        * volume.shape[4]
        / 8.0
    )
    grad_kernel = kernel_total / jnp.sqrt(jnp.float32(total_cells))
    return (activated, grad_input.astype(jnp.bfloat16), grad_kernel)


def solution(mesh):
    placed = (P("dp", None, "space", None, None), P(), P("dp", None, "space", None, None))
    return jax.shard_map(
        per_device,
        mesh=mesh,
        in_specs=placed,
        out_specs=(P("dp", None, "space", None, None), P("dp", None, "space", None, None), P()),
        check_vma=False,
    )
```

```python
import jax
import jax.numpy as jnp
from jax import lax
from jax.sharding import PartitionSpec as P


def from_behind(block, axis, distance):
    devices = range(lax.axis_size(axis))
    route = [(i - distance, i) for i in devices if i - distance in devices]
    return lax.ppermute(block, axis, route)


def in_blocks(x, dim, devices):
    dims = x.shape
    parts = x.reshape(*dims[:dim], devices, dims[dim] // devices, *dims[dim + 1 :])
    return jnp.moveaxis(parts, dim, 0)


def summed_on_arrival(x, axis, dim):
    parts = in_blocks(x, dim, lax.axis_size(axis))
    arrived = lax.all_to_all(parts.astype(jnp.bfloat16), axis, split_axis=0, concat_axis=0, tiled=True)
    return arrived.astype(jnp.float32).sum(axis=0)


def sent_to_all(x, axis):
    copies = jnp.broadcast_to(x, (lax.axis_size(axis), *x.shape))
    return lax.all_to_all(copies, axis, split_axis=0, concat_axis=0, tiled=True)


def taken_together(x, axis):
    everything = sent_to_all(x.astype(jnp.bfloat16), axis)
    return jnp.sum(everything.astype(jnp.float32), axis=0)


def laid_out(parts, dim):
    parts = jnp.moveaxis(parts, 0, dim)
    dims = parts.shape
    return parts.reshape(*dims[:dim], dims[dim] * dims[dim + 1], *dims[dim + 2 :])


def gathered_copies(x, axis, dim):
    parts = sent_to_all(x.astype(jnp.bfloat16), axis)
    return laid_out(parts.astype(jnp.float32), dim)


def convolve(inputs, weights, low, high):
    return lax.conv_general_dilated(
        inputs,
        weights,
        (2, 2, 2),
        [(low, high), (1, 1), (1, 1)],
        dimension_numbers=("NCDHW", "OIDHW", "NCDHW"),
        preferred_element_type=jnp.float32,
    )


def input_grad(grads, weights, low, high):
    flipped = weights[:, :, ::-1, ::-1, ::-1]
    return lax.conv_general_dilated(
        grads,
        flipped,
        (1, 1, 1),
        [(low, high), (1, 2), (1, 2)],
        lhs_dilation=(2, 2, 2),
        dimension_numbers=("NCDHW", "IODHW", "NCDHW"),
        preferred_element_type=jnp.float32,
    )


def weight_grad(inputs, grads):
    return lax.conv_general_dilated(
        inputs,
        grads,
        (1, 1, 1),
        [(0, 0), (1, 0), (1, 0)],
        rhs_dilation=(2, 2, 2),
        dimension_numbers=("CNDHW", "IODHW", "CNDHW"),
        preferred_element_type=jnp.float32,
    )


def per_device(volume, kernel, cotangent):
    below = from_behind(volume[:, :, -1:], "space", 1)
    extended = jnp.concatenate([below, volume], axis=2)
    pre = convolve(extended, kernel, 0, 0)
    activated = (0.01 * pre + 0.99 * jax.nn.softplus(pre)).astype(jnp.bfloat16)
    local_grad = (cotangent.astype(jnp.float32) * (0.01 + 0.99 * jax.nn.sigmoid(pre))).astype(
        jnp.bfloat16
    )
    grad_extended = input_grad(local_grad, kernel, 2, 2)
    kernel_local = weight_grad(extended, local_grad)
    grad_input = grad_extended[:, :, 1:]
    flat_terms = kernel_local.reshape(-1)
    share = summed_on_arrival(flat_terms, "space", 0)
    first_grad, share = lax.optimization_barrier((local_grad[:, :, :1], share))
    next_grad = from_behind(first_grad, "space", -1)
    from_above = input_grad(next_grad, kernel, 2, 0)
    grad_input = grad_input.at[:, :, -1:].add(from_above)
    share = taken_together(share, "dp")
    kernel_total = gathered_copies(share, "space", 0).reshape(kernel_local.shape)
    total_cells = (
        volume.shape[0]
        * lax.axis_size("dp")
        * volume.shape[2]
        * lax.axis_size("space")
        * volume.shape[3]
        * volume.shape[4]
        / 8.0
    )
    grad_kernel = kernel_total / jnp.sqrt(jnp.float32(total_cells))
    return (activated, grad_input.astype(jnp.bfloat16), grad_kernel)


def solution(mesh):
    placed = (P("dp", None, "space", None, None), P(), P("dp", None, "space", None, None))
    return jax.shard_map(
        per_device,
        mesh=mesh,
        in_specs=placed,
        out_specs=(P("dp", None, "space", None, None), P("dp", None, "space", None, None), P()),
        check_vma=False,
    )
```

```python
import jax
import jax.numpy as jnp
from jax import lax
from jax.sharding import PartitionSpec as P


def from_behind(block, axis, distance):
    devices = range(lax.axis_size(axis))
    route = [(i - distance, i) for i in devices if i - distance in devices]
    return lax.ppermute(block, axis, route)


def in_blocks(x, dim, devices):
    dims = x.shape
    parts = x.reshape(*dims[:dim], devices, dims[dim] // devices, *dims[dim + 1 :])
    return jnp.moveaxis(parts, dim, 0)


def summed_on_arrival(x, axis, dim):
    parts = in_blocks(x, dim, lax.axis_size(axis))
    arrived = lax.all_to_all(parts, axis, split_axis=0, concat_axis=0, tiled=True)
    return arrived.sum(axis=0)


def sent_to_all(x, axis):
    copies = jnp.broadcast_to(x, (lax.axis_size(axis), *x.shape))
    return lax.all_to_all(copies, axis, split_axis=0, concat_axis=0, tiled=True)


def taken_together(x, axis):
    everything = sent_to_all(x, axis)
    return jnp.sum(everything, axis=0)


def laid_out(parts, dim):
    parts = jnp.moveaxis(parts, 0, dim)
    dims = parts.shape
    return parts.reshape(*dims[:dim], dims[dim] * dims[dim + 1], *dims[dim + 2 :])


def gathered_copies(x, axis, dim):
    parts = sent_to_all(x.astype(jnp.bfloat16), axis)
    return laid_out(parts.astype(jnp.float32), dim)


def convolve(inputs, weights, low, high):
    return lax.conv_general_dilated(
        inputs,
        weights,
        (2, 2, 2),
        [(low, high), (1, 1), (1, 1)],
        dimension_numbers=("NCDHW", "OIDHW", "NCDHW"),
        preferred_element_type=jnp.float32,
    )


def input_grad(grads, weights, low, high):
    flipped = weights[:, :, ::-1, ::-1, ::-1]
    return lax.conv_general_dilated(
        grads,
        flipped,
        (1, 1, 1),
        [(low, high), (1, 2), (1, 2)],
        lhs_dilation=(2, 2, 2),
        dimension_numbers=("NCDHW", "IODHW", "NCDHW"),
        preferred_element_type=jnp.float32,
    )


def weight_grad(inputs, grads):
    return lax.conv_general_dilated(
        inputs,
        grads,
        (1, 1, 1),
        [(0, 0), (1, 0), (1, 0)],
        rhs_dilation=(2, 2, 2),
        dimension_numbers=("CNDHW", "IODHW", "CNDHW"),
        preferred_element_type=jnp.float32,
    )


def per_device(volume, kernel, cotangent):
    below = from_behind(volume[:, :, -1:], "space", 1)
    extended = jnp.concatenate([below, volume], axis=2)
    pre = convolve(extended, kernel, 0, 0)
    activated = (0.01 * pre + 0.99 * jax.nn.softplus(pre)).astype(jnp.bfloat16)
    local_grad = (cotangent.astype(jnp.float32) * (0.01 + 0.99 * jax.nn.sigmoid(pre))).astype(
        jnp.bfloat16
    )
    grad_extended = input_grad(local_grad, kernel, 2, 2)
    kernel_local = weight_grad(extended, local_grad)
    grad_input = grad_extended[:, :, 1:]
    next_grad = from_behind(local_grad[:, :, :1], "space", -1)
    from_above = input_grad(next_grad, kernel, 2, 0)
    grad_input = grad_input.at[:, :, -1:].add(from_above)
    flat_terms = kernel_local.reshape(-1)
    share = summed_on_arrival(flat_terms, "space", 0)
    share = taken_together(share, "dp")
    kernel_total = gathered_copies(share, "space", 0).reshape(kernel_local.shape)
    total_cells = (
        volume.shape[0]
        * lax.axis_size("dp")
        * volume.shape[2]
        * lax.axis_size("space")
        * volume.shape[3]
        * volume.shape[4]
        / 8.0
    )
    grad_kernel = kernel_total / jnp.sqrt(jnp.float32(total_cells))
    return (activated, grad_input.astype(jnp.bfloat16), grad_kernel)


def solution(mesh):
    placed = (P("dp", None, "space", None, None), P(), P("dp", None, "space", None, None))
    return jax.shard_map(
        per_device,
        mesh=mesh,
        in_specs=placed,
        out_specs=(P("dp", None, "space", None, None), P("dp", None, "space", None, None), P()),
        check_vma=False,
    )
```
